128 devices in a mesh: epoch: 8 (over z, y_hi), row: 16 (over y_lo, x, core).
Axes of the slice: x: 4, y: 4 (y_hi: 2, y_lo: 2; y = y_hi * 2 + y_lo), z: 4, core: 2. Of those that a mesh axis runs over, the one named last changes fastest.
Arguments:
- field: bfloat16 [1024, 512, 512], P('epoch', 'row'), may hold values from -6 to 6
- factor: bfloat16 [1024, 1024], P('epoch'), may hold values from -0.1875 to 0.1875
- kappa: float32 [512, 512], P('row'), may hold values from 0.05 to 1
Outputs:
- product: float32 [1024, 512, 512], P('epoch', 'row')
The draws below stay inside these ranges and needn't reach their ends.
All inputs are finite; a program needn't handle non-finite values.
Results may differ from the reference program's by a relative error of at most 0.0004.
Values may be sent and summed in bfloat16 or wider, within the bound.
No kernel may reach another device: no remote copies, remote signals or barrier semaphores. Data moves between devices by JAX's collectives and lax.ppermute only.
A program may use at most 192 MiB of HBM per device.

```python
import math
import jax
import jax.numpy as jnp
from jax import lax

EP_DEV = 128
NC = 512
NT = 1024
NR = 512
N_EPOCH = 8


def block_scale(rng, shape, cuts, low, largest):
    def one(position, parts):
        heights = jax.random.uniform(jax.random.fold_in(jax.random.fold_in(rng, 6), position), (parts,), jnp.float32, low / len(cuts), largest / len(cuts))
        return jnp.repeat(jnp.exp(heights), shape[position] // parts).reshape((-1,) + (1,) * (len(shape) - position - 1))

    loudness = one(*cuts[0])
    for cut in cuts[1:]:
        loudness = loudness * one(*cut)
    return loudness


def scatter_about(stream_key, extent, width, bound, cuts=(), kind=jnp.bfloat16):
    values = width * jax.random.normal(stream_key, extent, jnp.float32)
    if cuts:
        values = values * block_scale(stream_key, extent, cuts, -0.22, 0.18)
    return jnp.clip(values, -bound, bound).astype(kind)


def setup_inputs(seed: int = 0) -> dict:
    splits = jax.random.split(jax.random.key(seed), 4)
    field = scatter_about(splits[0], (NT, NR, NC), 1.0, 6.0, ((0, 8), (1, 16)))
    factor = scatter_about(splits[1], (NT, NT), NT ** -0.5, 0.1875, ((0, 8),))
    kappa = jnp.clip(jnp.exp(math.log(1.0) - 2.9957323 * jax.random.uniform(splits[2], (NR, NC), jnp.float32) ** block_scale(splits[2], (NR, NC), ((0, 16),), -0.2, 0.2)), 0.05, 1.0)
    return dict(field=field, factor=factor, kappa=kappa)


def operate(v, kappa):
    padded = jnp.pad(v, ((0, 0), (1, 1), (1, 1)))
    upper = padded[:, :-2, 1:-1]
    lower_rows = padded[:, 2:, 1:-1]
    left = padded[:, 1:-1, :-2]
    right = padded[:, 1:-1, 2:]
    return (kappa + 4.0) * v - (upper + lower_rows + left + right)


def reference(field, factor, kappa):
    rows = lax.broadcasted_iota(jnp.int32, (NT, NT), 0)
    cols = lax.broadcasted_iota(jnp.int32, (NT, NT), 1)
    lower = jnp.where(cols <= rows, factor, jnp.zeros_like(factor))
    flat = field.reshape(NT, NR * NC)

    def block(index):
        start = (index * EP_DEV).astype(jnp.int32)
        part_rows = lax.dynamic_slice_in_dim(lower, start, EP_DEV, 0)
        timed = jnp.dot(part_rows, flat, preferred_element_type=jnp.float32).reshape(EP_DEV, NR, NC)
        return operate(operate(timed, kappa), kappa)

    result = lax.map(block, jnp.arange(N_EPOCH, dtype=jnp.int32))
    return result.reshape(NT, NR, NC)
```

```python
import jax
import jax.numpy as jnp
from jax import lax
from jax.sharding import PartitionSpec as P


def with_halo(x, sides, width):
    for axis, dim in sides:
        size, length = (lax.axis_size(axis), x.shape[dim])
        up = [(i, (i + 1) % size) for i in range(size - 1)]
        down = [(j, i) for i, j in up]
        last = lax.slice_in_dim(x, length - width, length, axis=dim)
        first = lax.slice_in_dim(x, 0, width, axis=dim)
        before = lax.ppermute(last, axis, up)
        after = lax.ppermute(first, axis, down)
        x = jnp.concatenate([before, x, after], axis=dim)
    return x


def stencil(padded, kappa):
    center = padded[:, 1:-1, :]
    sides = jnp.pad(center, ((0, 0), (0, 0), (1, 1)))
    upper = padded[:, :-2, :]
    below = padded[:, 2:, :]
    return (kappa + 4.0) * center - (upper + below + sides[:, :, :-2] + sides[:, :, 2:])


def single_rim(values):
    return with_halo(values, (("row", 1),), 1)


def body(field, factor, kappa):
    epochs = field.shape[0]
    count = lax.axis_size("epoch")
    order = epochs * count
    me = lax.axis_index("epoch")
    global_rows = me * epochs + lax.broadcasted_iota(jnp.int32, (epochs, order), 0)
    global_cols = lax.broadcasted_iota(jnp.int32, (epochs, order), 1)
    lower = jnp.where(global_cols <= global_rows, factor, jnp.zeros_like(factor))
    own = jnp.transpose(field, (1, 2, 0))

    def term(block, source):
        start = jnp.clip(source, 0, count - 1) * epochs
        part = lax.dynamic_slice_in_dim(lower, start, epochs, 1)
        return jnp.einsum("ts,ijs->tij", part, block, preferred_element_type=jnp.float32)

    timed = term(own, me)
    for shift in range(1, count):
        pairs = [(e, e + shift) for e in range(count - shift)]
        got = lax.ppermute(own, "epoch", pairs)
        timed = timed + term(got, me - shift)
    first = stencil(single_rim(timed), kappa)
    return stencil(single_rim(first), kappa)


def solution(mesh):
    in_specs = (P("epoch", "row", None), P("epoch", None), P("row", None))
    out_specs = P("epoch", "row", None)
    return jax.shard_map(body, mesh=mesh, in_specs=in_specs, out_specs=out_specs, check_vma=False)
```

```python
import jax
import jax.numpy as jnp
from jax import lax
from jax.sharding import PartitionSpec as P

CHUNKS = 4


def with_halo(x, sides, width):
    for axis, dim in sides:
        size, length = (lax.axis_size(axis), x.shape[dim])
        up = [(i, (i + 1) % size) for i in range(size - 1)]
        down = [(j, i) for i, j in up]
        last = lax.slice_in_dim(x, length - width, length, axis=dim)
        first = lax.slice_in_dim(x, 0, width, axis=dim)
        before = lax.ppermute(last, axis, up)
        after = lax.ppermute(first, axis, down)
        x = jnp.concatenate([before, x, after], axis=dim)
    return x


def stencil(padded, kappa):
    center = padded[:, 1:-1, :]
    sides = jnp.pad(center, ((0, 0), (0, 0), (1, 1)))
    upper = padded[:, :-2, :]
    below = padded[:, 2:, :]
    return (kappa + 4.0) * center - (upper + below + sides[:, :, :-2] + sides[:, :, 2:])


def single_rim(values):
    return with_halo(values, (("row", 1),), 1)


def body(field, factor, kappa):
    epochs, slab, width = field.shape
    count = lax.axis_size("epoch")
    order = epochs * count
    me = lax.axis_index("epoch")
    global_rows = me * epochs + lax.broadcasted_iota(jnp.int32, (epochs, order), 0)
    global_cols = lax.broadcasted_iota(jnp.int32, (epochs, order), 1)
    lower = jnp.where(global_cols <= global_rows, factor, jnp.zeros_like(factor))
    lower = lower.reshape(epochs, count, epochs)
    step = slab // CHUNKS
    parts = []
    for c in range(CHUNKS):
        rows = lax.slice_in_dim(field, c * step, (c + 1) * step, axis=1)
        rows = jnp.transpose(rows, (1, 2, 0))
        got = lax.all_gather(rows, "epoch", axis=0)
        parts.append(
            jnp.einsum("tes,eijs->tij", lower, got, preferred_element_type=jnp.float32)
        )
    timed = jnp.concatenate(parts, axis=1)
    first = stencil(single_rim(timed), kappa)
    return stencil(single_rim(first), kappa)


def solution(mesh):
    in_specs = (P("epoch", "row", None), P("epoch", None), P("row", None))
    out_specs = P("epoch", "row", None)
    return jax.shard_map(body, mesh=mesh, in_specs=in_specs, out_specs=out_specs, check_vma=False)
```

```python
import jax
import jax.numpy as jnp
from jax import lax
from jax.sharding import PartitionSpec as P

GATHERED_ROWS = 16


def with_halo(x, sides, width):
    for axis, dim in sides:
        size, length = (lax.axis_size(axis), x.shape[dim])
        up = [(i, (i + 1) % size) for i in range(size - 1)]
        down = [(j, i) for i, j in up]
        last = lax.slice_in_dim(x, length - width, length, axis=dim)
        first = lax.slice_in_dim(x, 0, width, axis=dim)
        before = lax.ppermute(last, axis, up)
        after = lax.ppermute(first, axis, down)
        x = jnp.concatenate([before, x, after], axis=dim)
    return x


def stencil(padded, kappa):
    center = padded[:, 1:-1, :]
    sides = jnp.pad(center, ((0, 0), (0, 0), (1, 1)))
    upper = padded[:, :-2, :]
    below = padded[:, 2:, :]
    return (kappa + 4.0) * center - (upper + below + sides[:, :, :-2] + sides[:, :, 2:])


def single_rim(values):
    return with_halo(values, (("row", 1),), 1)


def body(field, factor, kappa):
    epochs, slab, width = field.shape
    count = lax.axis_size("epoch")
    order = epochs * count
    me = lax.axis_index("epoch")
    global_rows = me * epochs + lax.broadcasted_iota(jnp.int32, (epochs, order), 0)
    global_cols = lax.broadcasted_iota(jnp.int32, (epochs, order), 1)
    lower = jnp.where(global_cols <= global_rows, factor, jnp.zeros_like(factor))
    lower = lower.reshape(epochs, count, epochs)
    own = jnp.transpose(field, (1, 2, 0))
    head = own[:GATHERED_ROWS]
    tail = own[GATHERED_ROWS:]
    gathered = lax.all_gather(head, "epoch", axis=0)
    slots = [tail]
    for shift in range(1, count):
        pairs = [(e, e + shift) for e in range(count - shift)]
        slots.append(lax.ppermute(tail, "epoch", pairs))
    stacked = jnp.stack(slots, axis=0)
    source = jnp.clip(me - jnp.arange(count), 0, count - 1)
    weights = jnp.take(lower, source, axis=1)
    part_a = jnp.einsum("tes,eijs->tij", lower, gathered, preferred_element_type=jnp.float32)
    part_b = jnp.einsum("tes,eijs->tij", weights, stacked, preferred_element_type=jnp.float32)
    timed = jnp.concatenate([part_a, part_b], axis=1)
    first = stencil(single_rim(timed), kappa)
    return stencil(single_rim(first), kappa)


def solution(mesh):
    in_specs = (P("epoch", "row", None), P("epoch", None), P("row", None))
    out_specs = P("epoch", "row", None)
    return jax.shard_map(body, mesh=mesh, in_specs=in_specs, out_specs=out_specs, check_vma=False)
```

```python
import jax
import jax.numpy as jnp
from jax import lax
from jax.sharding import PartitionSpec as P

GATHERED_ROWS = 16
HALO = 2


def neighbours(x, width):
    size = lax.axis_size("row")
    up = [(i, i + 1) for i in range(size - 1)]
    down = [(i + 1, i) for i in range(size - 1)]
    above = lax.ppermute(x[x.shape[0] - width:], "row", up)
    below = lax.ppermute(x[:width], "row", down)
    return above, below


def side_sum(v):
    padded = jnp.pad(v, [(0, 0)] * (v.ndim - 1) + [(1, 1)])
    return padded[..., :-2] + padded[..., 2:]


def body(field, factor, kappa):
    epochs, slab, width = field.shape
    count = lax.axis_size("epoch")
    order = epochs * count
    me = lax.axis_index("epoch")
    global_rows = me * epochs + lax.broadcasted_iota(jnp.int32, (epochs, order), 0)
    global_cols = lax.broadcasted_iota(jnp.int32, (epochs, order), 1)
    lower = jnp.where(global_cols <= global_rows, factor, jnp.zeros_like(factor))
    lower = lower.reshape(epochs, count, epochs)
    own = jnp.transpose(field, (1, 2, 0))
    head = own[:GATHERED_ROWS]
    tail = own[GATHERED_ROWS:]
    gathered = lax.all_gather(head, "epoch", axis=0)
    slots = [tail]
    for shift in range(1, count):
        pairs = [(e, e + shift) for e in range(count - shift)]
        slots.append(lax.ppermute(tail, "epoch", pairs))
    stacked = jnp.stack(slots, axis=0)
    source = jnp.clip(me - jnp.arange(count), 0, count - 1)
    weights = jnp.take(lower, source, axis=1)
    part_a = jnp.einsum("tes,eijs->itj", lower, gathered, preferred_element_type=jnp.float32)
    part_b = jnp.einsum("tes,eijs->itj", weights, stacked, preferred_element_type=jnp.float32)
    timed = jnp.concatenate([part_a, part_b], axis=0)

    above, below = neighbours(timed, HALO)
    k_above, k_below = neighbours(kappa, 1)
    ext = jnp.concatenate([above, timed, below], axis=0)
    gain = jnp.concatenate([k_above, kappa, k_below], axis=0)[:, None, :] + 4.0
    once = gain * ext[1:-1] - (ext[:-2] + ext[2:] + side_sum(ext[1:-1]))
    pos = lax.axis_index("row")
    rows = lax.broadcasted_iota(jnp.int32, (slab + 2, 1, 1), 0)
    outside = ((rows == 0) & (pos == 0)) | ((rows == slab + 1) & (pos == lax.axis_size("row") - 1))
    once = jnp.where(outside, jnp.zeros_like(once), once)
    product = gain[1:-1] * once[1:-1] - (once[:-2] + once[2:] + side_sum(once[1:-1]))
    return jnp.transpose(product, (1, 0, 2))


def solution(mesh):
    in_specs = (P("epoch", "row", None), P("epoch", None), P("row", None))
    out_specs = P("epoch", "row", None)
    return jax.shard_map(body, mesh=mesh, in_specs=in_specs, out_specs=out_specs, check_vma=False)
```

```python
import jax
import jax.numpy as jnp
from jax import lax
from jax.sharding import PartitionSpec as P

GATHERED_ROWS = 16
HALO = 2


def neighbours(x, width):
    size = lax.axis_size("row")
    up = [(i, i + 1) for i in range(size - 1)]
    down = [(i + 1, i) for i in range(size - 1)]
    above = lax.ppermute(x[x.shape[0] - width:], "row", up)
    below = lax.ppermute(x[:width], "row", down)
    return above, below


def side_sum(v):
    padded = jnp.pad(v, [(0, 0)] * (v.ndim - 1) + [(1, 1)])
    return padded[..., :-2] + padded[..., 2:]


def body(field, factor, kappa):
    epochs, slab, width = field.shape
    count = lax.axis_size("epoch")
    order = epochs * count
    me = lax.axis_index("epoch")
    global_rows = me * epochs + lax.broadcasted_iota(jnp.int32, (epochs, order), 0)
    global_cols = lax.broadcasted_iota(jnp.int32, (epochs, order), 1)
    lower = jnp.where(global_cols <= global_rows, factor, jnp.zeros_like(factor))
    lower = lower.reshape(epochs, count, epochs)
    own = jnp.transpose(field, (1, 2, 0))
    head = own[:GATHERED_ROWS]
    tail = own[GATHERED_ROWS:]
    gathered = lax.all_gather(head, "epoch", axis=0)
    a, b = count - 2, count - 1
    skip = {(e, b) for e in range(a) if e % 2 == a % 2} | {(e, a) for e in range(a) if e % 2 == b % 2}
    slots = [tail]
    for shift in range(1, count):
        pairs = [(e, e + shift) for e in range(count - shift) if (e, e + shift) not in skip]
        slots.append(lax.ppermute(tail, "epoch", pairs) if pairs else jnp.zeros_like(tail))
    relay = list(range(2, a + 1, 2))
    swapped = lax.ppermute(jnp.stack([slots[k] for k in relay]), "epoch", [(a, b), (b, a)])
    for m, k in enumerate(relay):
        at_a, at_b = k - 1, k + 1
        slots[at_a] = jnp.where(me == a, swapped[m], slots[at_a])
        slots[at_b] = jnp.where(me == b, swapped[m], slots[at_b])
    stacked = jnp.stack(slots, axis=0)
    source = jnp.clip(me - jnp.arange(count), 0, count - 1)
    weights = jnp.take(lower, source, axis=1)
    part_a = jnp.einsum("tes,eijs->itj", lower, gathered, preferred_element_type=jnp.float32)
    part_b = jnp.einsum("tes,eijs->itj", weights, stacked, preferred_element_type=jnp.float32)
    timed = jnp.concatenate([part_a, part_b], axis=0)

    above, below = neighbours(timed, HALO)
    k_above, k_below = neighbours(kappa, 1)
    ext = jnp.concatenate([above, timed, below], axis=0)
    gain = jnp.concatenate([k_above, kappa, k_below], axis=0)[:, None, :] + 4.0
    once = gain * ext[1:-1] - (ext[:-2] + ext[2:] + side_sum(ext[1:-1]))
    pos = lax.axis_index("row")
    rows = lax.broadcasted_iota(jnp.int32, (slab + 2, 1, 1), 0)
    outside = ((rows == 0) & (pos == 0)) | ((rows == slab + 1) & (pos == lax.axis_size("row") - 1))
    once = jnp.where(outside, jnp.zeros_like(once), once)
    product = gain[1:-1] * once[1:-1] - (once[:-2] + once[2:] + side_sum(once[1:-1]))
    return jnp.transpose(product, (1, 0, 2))


def solution(mesh):
    in_specs = (P("epoch", "row", None), P("epoch", None), P("row", None))
    out_specs = P("epoch", "row", None)
    return jax.shard_map(body, mesh=mesh, in_specs=in_specs, out_specs=out_specs, check_vma=False)
```

```python
import jax
import jax.numpy as jnp
from jax import lax
from jax.sharding import PartitionSpec as P

EDGE = 8
HALO = 2


def neighbours(top, bottom, width):
    size = lax.axis_size("row")
    up = [(i, i + 1) for i in range(size - 1)]
    down = [(i + 1, i) for i in range(size - 1)]
    above = lax.ppermute(bottom[bottom.shape[0] - width:], "row", up)
    below = lax.ppermute(top[:width], "row", down)
    return above, below


def side_sum(v):
    padded = jnp.pad(v, [(0, 0)] * (v.ndim - 1) + [(1, 1)])
    return padded[..., :-2] + padded[..., 2:]


def double_stencil(ext, gain_once, gain_out, first_outside=None, last_outside=None):
    once = gain_once * ext[1:-1] - (ext[:-2] + ext[2:] + side_sum(ext[1:-1]))
    if first_outside is not None or last_outside is not None:
        rows = lax.broadcasted_iota(jnp.int32, (once.shape[0], 1, 1), 0)
        outside = jnp.zeros(rows.shape, jnp.bool_)
        if first_outside is not None:
            outside = outside | ((rows == 0) & first_outside)
        if last_outside is not None:
            outside = outside | ((rows == once.shape[0] - 1) & last_outside)
        once = jnp.where(outside, jnp.zeros_like(once), once)
    return gain_out * once[1:-1] - (once[:-2] + once[2:] + side_sum(once[1:-1]))


def body(field, factor, kappa):
    epochs, slab, width = field.shape
    count = lax.axis_size("epoch")
    order = epochs * count
    me = lax.axis_index("epoch")
    global_rows = me * epochs + lax.broadcasted_iota(jnp.int32, (epochs, order), 0)
    global_cols = lax.broadcasted_iota(jnp.int32, (epochs, order), 1)
    lower = jnp.where(global_cols <= global_rows, factor, jnp.zeros_like(factor))
    lower = lower.reshape(epochs, count, epochs)
    middle = jnp.transpose(field[:, EDGE:slab - EDGE], (1, 2, 0))
    gathered = lax.all_gather(middle, "epoch", axis=0)
    edges = jnp.transpose(
        jnp.concatenate([field[:, :EDGE], field[:, slab - EDGE:]], axis=1), (1, 2, 0)
    )
    slots = [edges]
    for shift in range(1, count):
        pairs = [(e, e + shift) for e in range(count - shift)]
        slots.append(lax.ppermute(edges, "epoch", pairs))
    stacked = jnp.stack(slots, axis=0)
    source = jnp.clip(me - jnp.arange(count), 0, count - 1)
    weights = jnp.take(lower, source, axis=1)
    timed_edges = jnp.einsum("tes,eijs->itj", weights, stacked, preferred_element_type=jnp.float32)
    top, bottom = timed_edges[:EDGE], timed_edges[EDGE:]

    above, below = neighbours(top, bottom, HALO)
    k_above, k_below = neighbours(kappa, kappa, 1)
    gain = jnp.concatenate([k_above, kappa, k_below], axis=0)[:, None, :] + 4.0
    pos = lax.axis_index("row")
    last = lax.axis_size("row") - 1
    out_top = double_stencil(
        jnp.concatenate([above, top], axis=0),
        gain[0:EDGE], gain[1:EDGE - 1], first_outside=pos == 0,
    )
    out_bottom = double_stencil(
        jnp.concatenate([bottom, below], axis=0),
        gain[slab - EDGE + 2:slab + 2], gain[slab - EDGE + 3:slab + 1], last_outside=pos == last,
    )
    timed_middle = jnp.einsum("tes,eijs->itj", lower, gathered, preferred_element_type=jnp.float32)
    ext = jnp.concatenate([top[EDGE - 2 * HALO:], timed_middle, bottom[:2 * HALO]], axis=0)
    out_middle = double_stencil(ext, gain[EDGE - 2:slab - EDGE + 4], gain[EDGE - 1:slab - EDGE + 3])
    product = jnp.concatenate([out_top, out_middle, out_bottom], axis=0)
    return jnp.transpose(product, (1, 0, 2))


def solution(mesh):
    in_specs = (P("epoch", "row", None), P("epoch", None), P("row", None))
    out_specs = P("epoch", "row", None)
    return jax.shard_map(body, mesh=mesh, in_specs=in_specs, out_specs=out_specs, check_vma=False)
```

```python
import jax
import jax.numpy as jnp
from jax import lax
from jax.sharding import PartitionSpec as P

EDGE = 12
HALO = 2


def neighbours(top, bottom, width):
    size = lax.axis_size("row")
    up = [(i, i + 1) for i in range(size - 1)]
    down = [(i + 1, i) for i in range(size - 1)]
    above = lax.ppermute(bottom[bottom.shape[0] - width:], "row", up)
    below = lax.ppermute(top[:width], "row", down)
    return above, below


def side_sum(v):
    padded = jnp.pad(v, [(0, 0)] * (v.ndim - 1) + [(1, 1)])
    return padded[..., :-2] + padded[..., 2:]


def double_stencil(ext, gain_once, gain_out, first_outside=None, last_outside=None):
    once = gain_once * ext[1:-1] - (ext[:-2] + ext[2:] + side_sum(ext[1:-1]))
    if first_outside is not None or last_outside is not None:
        rows = lax.broadcasted_iota(jnp.int32, (once.shape[0], 1, 1), 0)
        outside = jnp.zeros(rows.shape, jnp.bool_)
        if first_outside is not None:
            outside = outside | ((rows == 0) & first_outside)
        if last_outside is not None:
            outside = outside | ((rows == once.shape[0] - 1) & last_outside)
        once = jnp.where(outside, jnp.zeros_like(once), once)
    return gain_out * once[1:-1] - (once[:-2] + once[2:] + side_sum(once[1:-1]))


def body(field, factor, kappa):
    epochs, slab, width = field.shape
    count = lax.axis_size("epoch")
    order = epochs * count
    me = lax.axis_index("epoch")
    global_rows = me * epochs + lax.broadcasted_iota(jnp.int32, (epochs, order), 0)
    global_cols = lax.broadcasted_iota(jnp.int32, (epochs, order), 1)
    lower = jnp.where(global_cols <= global_rows, factor, jnp.zeros_like(factor))
    lower = lower.reshape(epochs, count, epochs)
    middle = jnp.transpose(field[:, EDGE:slab - EDGE], (1, 2, 0))
    gathered = lax.all_gather(middle, "epoch", axis=0)
    edges = jnp.transpose(
        jnp.concatenate([field[:, :EDGE], field[:, slab - EDGE:]], axis=1), (1, 2, 0)
    )
    slots = [edges]
    for shift in range(1, count):
        pairs = [(e, e + shift) for e in range(count - shift)]
        slots.append(lax.ppermute(edges, "epoch", pairs))
    stacked = jnp.stack(slots, axis=0)
    source = jnp.clip(me - jnp.arange(count), 0, count - 1)
    weights = jnp.take(lower, source, axis=1)
    timed_edges = jnp.einsum("tes,eijs->itj", weights, stacked, preferred_element_type=jnp.float32)
    top, bottom = timed_edges[:EDGE], timed_edges[EDGE:]

    above, below = neighbours(top, bottom, HALO)
    k_above, k_below = neighbours(kappa, kappa, 1)
    gain = jnp.concatenate([k_above, kappa, k_below], axis=0)[:, None, :] + 4.0
    pos = lax.axis_index("row")
    last = lax.axis_size("row") - 1
    out_top = double_stencil(
        jnp.concatenate([above, top], axis=0),
        gain[0:EDGE], gain[1:EDGE - 1], first_outside=pos == 0,
    )
    out_bottom = double_stencil(
        jnp.concatenate([bottom, below], axis=0),
        gain[slab - EDGE + 2:slab + 2], gain[slab - EDGE + 3:slab + 1], last_outside=pos == last,
    )
    timed_middle = jnp.einsum("tes,eijs->itj", lower, gathered, preferred_element_type=jnp.float32)
    ext = jnp.concatenate([top[EDGE - 2 * HALO:], timed_middle, bottom[:2 * HALO]], axis=0)
    out_middle = double_stencil(ext, gain[EDGE - 2:slab - EDGE + 4], gain[EDGE - 1:slab - EDGE + 3])
    product = jnp.concatenate([out_top, out_middle, out_bottom], axis=0)
    return jnp.transpose(product, (1, 0, 2))


def solution(mesh):
    in_specs = (P("epoch", "row", None), P("epoch", None), P("row", None))
    out_specs = P("epoch", "row", None)
    return jax.shard_map(body, mesh=mesh, in_specs=in_specs, out_specs=out_specs, check_vma=False)
```

```python
import jax
import jax.numpy as jnp
from jax import lax
from jax.sharding import PartitionSpec as P

EDGE = 8
HALO = 2


def neighbours(top, bottom, width):
    size = lax.axis_size("row")
    up = [(i, i + 1) for i in range(size - 1)]
    down = [(i + 1, i) for i in range(size - 1)]
    above = lax.ppermute(bottom[bottom.shape[0] - width:], "row", up)
    below = lax.ppermute(top[:width], "row", down)
    return above, below


def side_sum(v):
    padded = jnp.pad(v, [(0, 0)] * (v.ndim - 1) + [(1, 1)])
    return padded[..., :-2] + padded[..., 2:]


def double_stencil(ext, gain_once, gain_out, first_outside=None, last_outside=None):
    once = gain_once * ext[1:-1] - (ext[:-2] + ext[2:] + side_sum(ext[1:-1]))
    if first_outside is not None or last_outside is not None:
        rows = lax.broadcasted_iota(jnp.int32, (once.shape[0], 1, 1), 0)
        outside = jnp.zeros(rows.shape, jnp.bool_)
        if first_outside is not None:
            outside = outside | ((rows == 0) & first_outside)
        if last_outside is not None:
            outside = outside | ((rows == once.shape[0] - 1) & last_outside)
        once = jnp.where(outside, jnp.zeros_like(once), once)
    return gain_out * once[1:-1] - (once[:-2] + once[2:] + side_sum(once[1:-1]))


def body(field, factor, kappa):
    epochs, slab, width = field.shape
    count = lax.axis_size("epoch")
    order = epochs * count
    me = lax.axis_index("epoch")
    global_rows = me * epochs + lax.broadcasted_iota(jnp.int32, (epochs, order), 0)
    global_cols = lax.broadcasted_iota(jnp.int32, (epochs, order), 1)
    lower = jnp.where(global_cols <= global_rows, factor, jnp.zeros_like(factor))
    lower = lower.reshape(epochs, count, epochs)
    middle = jnp.transpose(field[:, EDGE:slab - EDGE], (1, 2, 0))
    gathered = lax.all_gather(middle, "epoch", axis=0)
    edges = jnp.transpose(
        jnp.concatenate([field[:, :EDGE], field[:, slab - EDGE:]], axis=1), (1, 2, 0)
    )
    a, b = count - 2, count - 1
    p, q = count - 4, count - 3
    slots = [edges]
    for shift in range(1, count):
        pairs = [(e, e + shift) for e in range(count - shift) if e + shift < a or e == a]
        slots.append(lax.ppermute(edges, "epoch", pairs))
    stacked = jnp.stack(slots, axis=0)
    source = jnp.clip(me - jnp.arange(count), 0, count - 1)
    weights = jnp.take(lower, source, axis=1)
    timed_edges = jnp.einsum("tes,eijs->itj", weights, stacked, preferred_element_type=jnp.float32)
    extra = lax.ppermute(edges, "epoch", [(q, p)])
    target = lax.ppermute(lower, "epoch", [(a, p), (b, q)])
    partial = jnp.einsum(
        "tes,eijs->itj", jnp.take(target, source, axis=1), stacked, preferred_element_type=jnp.float32
    )
    above_block = lax.dynamic_index_in_dim(target, jnp.clip(me + 1, 0, count - 1), 1, keepdims=False)
    partial = partial + jnp.einsum("ts,ijs->itj", above_block, extra, preferred_element_type=jnp.float32)
    timed_edges = timed_edges + lax.ppermute(partial, "epoch", [(p, a), (q, b)])
    top, bottom = timed_edges[:EDGE], timed_edges[EDGE:]

    above, below = neighbours(top, bottom, HALO)
    k_above, k_below = neighbours(kappa, kappa, 1)
    gain = jnp.concatenate([k_above, kappa, k_below], axis=0)[:, None, :] + 4.0
    pos = lax.axis_index("row")
    last = lax.axis_size("row") - 1
    out_top = double_stencil(
        jnp.concatenate([above, top], axis=0),
        gain[0:EDGE], gain[1:EDGE - 1], first_outside=pos == 0,
    )
    out_bottom = double_stencil(
        jnp.concatenate([bottom, below], axis=0),
        gain[slab - EDGE + 2:slab + 2], gain[slab - EDGE + 3:slab + 1], last_outside=pos == last,
    )
    timed_middle = jnp.einsum("tes,eijs->itj", lower, gathered, preferred_element_type=jnp.float32)
    ext = jnp.concatenate([top[EDGE - 2 * HALO:], timed_middle, bottom[:2 * HALO]], axis=0)
    out_middle = double_stencil(ext, gain[EDGE - 2:slab - EDGE + 4], gain[EDGE - 1:slab - EDGE + 3])
    product = jnp.concatenate([out_top, out_middle, out_bottom], axis=0)
    return jnp.transpose(product, (1, 0, 2))


def solution(mesh):
    in_specs = (P("epoch", "row", None), P("epoch", None), P("row", None))
    out_specs = P("epoch", "row", None)
    return jax.shard_map(body, mesh=mesh, in_specs=in_specs, out_specs=out_specs, check_vma=False)
```

```python
import jax
import jax.numpy as jnp
from jax import lax
from jax.sharding import PartitionSpec as P

EDGE = 10
HALO = 2


def neighbours(top, bottom, width):
    size = lax.axis_size("row")
    up = [(i, i + 1) for i in range(size - 1)]
    down = [(i + 1, i) for i in range(size - 1)]
    above = lax.ppermute(bottom[bottom.shape[0] - width:], "row", up)
    below = lax.ppermute(top[:width], "row", down)
    return above, below


def side_sum(v):
    padded = jnp.pad(v, [(0, 0)] * (v.ndim - 1) + [(1, 1)])
    return padded[..., :-2] + padded[..., 2:]


def double_stencil(ext, gain_once, gain_out, first_outside=None, last_outside=None):
    once = gain_once * ext[1:-1] - (ext[:-2] + ext[2:] + side_sum(ext[1:-1]))
    if first_outside is not None or last_outside is not None:
        rows = lax.broadcasted_iota(jnp.int32, (once.shape[0], 1, 1), 0)
        outside = jnp.zeros(rows.shape, jnp.bool_)
        if first_outside is not None:
            outside = outside | ((rows == 0) & first_outside)
        if last_outside is not None:
            outside = outside | ((rows == once.shape[0] - 1) & last_outside)
        once = jnp.where(outside, jnp.zeros_like(once), once)
    return gain_out * once[1:-1] - (once[:-2] + once[2:] + side_sum(once[1:-1]))


def body(field, factor, kappa):
    epochs, slab, width = field.shape
    count = lax.axis_size("epoch")
    order = epochs * count
    me = lax.axis_index("epoch")
    global_rows = me * epochs + lax.broadcasted_iota(jnp.int32, (epochs, order), 0)
    global_cols = lax.broadcasted_iota(jnp.int32, (epochs, order), 1)
    lower = jnp.where(global_cols <= global_rows, factor, jnp.zeros_like(factor))
    lower = lower.reshape(epochs, count, epochs)
    middle = jnp.transpose(field[:, EDGE:slab - EDGE], (1, 2, 0))
    gathered = lax.all_gather(middle, "epoch", axis=0)
    edges = jnp.transpose(
        jnp.concatenate([field[:, :EDGE], field[:, slab - EDGE:]], axis=1), (1, 2, 0)
    )
    slots = [edges]
    for shift in range(1, count):
        pairs = [(e, e + shift) for e in range(count - shift)]
        slots.append(lax.ppermute(edges, "epoch", pairs))
    stacked = jnp.stack(slots, axis=0)
    source = jnp.clip(me - jnp.arange(count), 0, count - 1)
    weights = jnp.take(lower, source, axis=1)
    timed_edges = jnp.einsum("tes,eijs->itj", weights, stacked, preferred_element_type=jnp.float32)
    top, bottom = timed_edges[:EDGE], timed_edges[EDGE:]

    above, below = neighbours(top, bottom, HALO)
    k_above, k_below = neighbours(kappa, kappa, 1)
    gain = jnp.concatenate([k_above, kappa, k_below], axis=0)[:, None, :] + 4.0
    pos = lax.axis_index("row")
    last = lax.axis_size("row") - 1
    out_top = double_stencil(
        jnp.concatenate([above, top], axis=0),
        gain[0:EDGE], gain[1:EDGE - 1], first_outside=pos == 0,
    )
    out_bottom = double_stencil(
        jnp.concatenate([bottom, below], axis=0),
        gain[slab - EDGE + 2:slab + 2], gain[slab - EDGE + 3:slab + 1], last_outside=pos == last,
    )
    timed_middle = jnp.einsum("tes,eijs->itj", lower, gathered, preferred_element_type=jnp.float32)
    ext = jnp.concatenate([top[EDGE - 2 * HALO:], timed_middle, bottom[:2 * HALO]], axis=0)
    out_middle = double_stencil(ext, gain[EDGE - 2:slab - EDGE + 4], gain[EDGE - 1:slab - EDGE + 3])
    product = jnp.concatenate([out_top, out_middle, out_bottom], axis=0)
    return jnp.transpose(product, (1, 0, 2))


def solution(mesh):
    in_specs = (P("epoch", "row", None), P("epoch", None), P("row", None))
    out_specs = P("epoch", "row", None)
    return jax.shard_map(body, mesh=mesh, in_specs=in_specs, out_specs=out_specs, check_vma=False)
```

```python
import jax
import jax.numpy as jnp
from jax import lax
from jax.sharding import PartitionSpec as P

EDGE = 8
HALO = 2


def neighbours(top, bottom, width):
    size = lax.axis_size("row")
    up = [(i, i + 1) for i in range(size - 1)]
    down = [(i + 1, i) for i in range(size - 1)]
    above = lax.ppermute(bottom[bottom.shape[0] - width:], "row", up)
    below = lax.ppermute(top[:width], "row", down)
    return above, below


def side_sum(v):
    padded = jnp.pad(v, [(0, 0)] * (v.ndim - 1) + [(1, 1)])
    return padded[..., :-2] + padded[..., 2:]


def double_stencil(ext, gain_once, gain_out, first_outside=None, last_outside=None):
    once = gain_once * ext[1:-1] - (ext[:-2] + ext[2:] + side_sum(ext[1:-1]))
    if first_outside is not None or last_outside is not None:
        rows = lax.broadcasted_iota(jnp.int32, (once.shape[0], 1, 1), 0)
        outside = jnp.zeros(rows.shape, jnp.bool_)
        if first_outside is not None:
            outside = outside | ((rows == 0) & first_outside)
        if last_outside is not None:
            outside = outside | ((rows == once.shape[0] - 1) & last_outside)
        once = jnp.where(outside, jnp.zeros_like(once), once)
    return gain_out * once[1:-1] - (once[:-2] + once[2:] + side_sum(once[1:-1]))


def body(field, factor, kappa):
    epochs, slab, width = field.shape
    count = lax.axis_size("epoch")
    order = epochs * count
    me = lax.axis_index("epoch")
    global_rows = me * epochs + lax.broadcasted_iota(jnp.int32, (epochs, order), 0)
    global_cols = lax.broadcasted_iota(jnp.int32, (epochs, order), 1)
    lower = jnp.where(global_cols <= global_rows, factor, jnp.zeros_like(factor))
    lower = lower.reshape(epochs, count, epochs)
    middle = jnp.transpose(field[:, EDGE:slab - EDGE], (1, 2, 0))
    gathered = lax.all_gather(middle, "epoch", axis=0)
    edges = jnp.transpose(
        jnp.concatenate([field[:, :EDGE], field[:, slab - EDGE:]], axis=1), (1, 2, 0)
    )
    a, b = count - 2, count - 1
    p, q = a - 4, b - 4
    r, s = a - 6, b - 6
    slots = [edges]
    for shift in range(1, count):
        pairs = [(e, e + shift) for e in range(count - shift) if not (e + shift >= a and e <= q)]
        slots.append(lax.ppermute(edges, "epoch", pairs))
    stacked = jnp.stack(slots, axis=0)
    source = jnp.clip(me - jnp.arange(count), 0, count - 1)
    weights = jnp.take(lower, source, axis=1)
    timed_edges = jnp.einsum("tes,eijs->itj", weights, stacked, preferred_element_type=jnp.float32)
    extra = lax.ppermute(edges, "epoch", [(q, p)])
    target = lax.ppermute(lower, "epoch", [(a, p), (b, q)])
    near = q - p + 3
    partial = jnp.einsum(
        "tes,eijs->itj",
        jnp.take(target, source[:near], axis=1),
        jnp.stack(slots[:near], axis=0),
        preferred_element_type=jnp.float32,
    )
    above_block = lax.dynamic_index_in_dim(target, jnp.clip(me + 1, 0, count - 1), 1, keepdims=False)
    partial = partial + jnp.einsum("ts,ijs->itj", above_block, extra, preferred_element_type=jnp.float32)
    relayed = lax.ppermute(partial, "epoch", [(p, r), (q, s)])
    timed_edges = timed_edges + lax.ppermute(relayed, "epoch", [(r, a), (s, b)])
    top, bottom = timed_edges[:EDGE], timed_edges[EDGE:]

    above, below = neighbours(top, bottom, HALO)
    k_above, k_below = neighbours(kappa, kappa, 1)
    gain = jnp.concatenate([k_above, kappa, k_below], axis=0)[:, None, :] + 4.0
    pos = lax.axis_index("row")
    last = lax.axis_size("row") - 1
    out_top = double_stencil(
        jnp.concatenate([above, top], axis=0),
        gain[0:EDGE], gain[1:EDGE - 1], first_outside=pos == 0,
    )
    out_bottom = double_stencil(
        jnp.concatenate([bottom, below], axis=0),
        gain[slab - EDGE + 2:slab + 2], gain[slab - EDGE + 3:slab + 1], last_outside=pos == last,
    )
    timed_middle = jnp.einsum("tes,eijs->itj", lower, gathered, preferred_element_type=jnp.float32)
    ext = jnp.concatenate([top[EDGE - 2 * HALO:], timed_middle, bottom[:2 * HALO]], axis=0)
    out_middle = double_stencil(ext, gain[EDGE - 2:slab - EDGE + 4], gain[EDGE - 1:slab - EDGE + 3])
    product = jnp.concatenate([out_top, out_middle, out_bottom], axis=0)
    return jnp.transpose(product, (1, 0, 2))


def solution(mesh):
    in_specs = (P("epoch", "row", None), P("epoch", None), P("row", None))
    out_specs = P("epoch", "row", None)
    return jax.shard_map(body, mesh=mesh, in_specs=in_specs, out_specs=out_specs, check_vma=False)
```

```python
import jax
import jax.numpy as jnp
from jax import lax
from jax.experimental import pallas as pl
from jax.experimental.pallas import tpu as pltpu
from jax.sharding import PartitionSpec as P

EDGE = 8
HALO = 2


def neighbours(top, bottom, width):
    size = lax.axis_size("row")
    up = [(i, i + 1) for i in range(size - 1)]
    down = [(i + 1, i) for i in range(size - 1)]
    above = lax.ppermute(bottom[bottom.shape[0] - width:], "row", up)
    below = lax.ppermute(top[:width], "row", down)
    return above, below


def side_sum(v):
    padded = jnp.pad(v, [(0, 0)] * (v.ndim - 1) + [(1, 1)])
    return padded[..., :-2] + padded[..., 2:]


def double_stencil(ext, gain_once, gain_out, first_outside=None, last_outside=None):
    once = gain_once * ext[1:-1] - (ext[:-2] + ext[2:] + side_sum(ext[1:-1]))
    if first_outside is not None or last_outside is not None:
        rows = lax.broadcasted_iota(jnp.int32, (once.shape[0], 1, 1), 0)
        outside = jnp.zeros(rows.shape, jnp.bool_)
        if first_outside is not None:
            outside = outside | ((rows == 0) & first_outside)
        if last_outside is not None:
            outside = outside | ((rows == once.shape[0] - 1) & last_outside)
        once = jnp.where(outside, jnp.zeros_like(once), once)
    return gain_out * once[1:-1] - (once[:-2] + once[2:] + side_sum(once[1:-1]))


def _side(v):
    width = v.shape[-1]
    wrapped = pltpu.roll(v, 1, 1) + pltpu.roll(v, width - 1, 1)
    lanes = lax.broadcasted_iota(jnp.int32, v.shape, 1)
    first = jnp.broadcast_to(v[:, 0:1], v.shape)
    last = jnp.broadcast_to(v[:, width - 1:width], v.shape)
    wrapped = jnp.where(lanes == 0, wrapped - last, wrapped)
    return jnp.where(lanes == width - 1, wrapped - first, wrapped)


def _middle_kernel(lower_ref, g_ref, top_ref, bot_ref, gain_ref, out_ref, ext_ref, once_ref):
    i = pl.program_id(0)
    steps = pl.num_programs(0)
    halo = top_ref.shape[0]
    acc = jnp.zeros(out_ref.shape[1:], jnp.float32)
    for e in range(lower_ref.shape[0]):
        acc = acc + lax.dot_general(
            lower_ref[e], g_ref[e], (((1,), (1,)), ((), ())), preferred_element_type=jnp.float32
        )
    ext_ref[halo + i] = acc

    @pl.when(i == steps - 1)
    def _():
        rows = ext_ref.shape[0]
        for r in range(halo):
            ext_ref[r] = top_ref[r]
            ext_ref[rows - halo + r] = bot_ref[r]

        def once_row(r, carry):
            c = ext_ref[r + 1]
            once_ref[r] = gain_ref[r] * c - (ext_ref[r] + ext_ref[r + 2] + _side(c))
            return carry

        lax.fori_loop(0, rows - 2, once_row, 0)

        def out_row(r, carry):
            c = once_ref[r + 1]
            out_ref[r] = gain_ref[r + 1] * c - (once_ref[r] + once_ref[r + 2] + _side(c))
            return carry

        lax.fori_loop(0, rows - 4, out_row, 0)


def _pin_kernel(x_ref, o_ref):
    o_ref[...] = x_ref[...]


def pinned(x):
    return pl.pallas_call(_pin_kernel, out_shape=jax.ShapeDtypeStruct(x.shape, x.dtype))(x)


def middle_stencil(lower_e, gathered, top, bottom, gain_rows):
    count, epochs, _ = lower_e.shape
    _, rows, width, _ = gathered.shape
    halo = top.shape[0]
    ext_rows = rows + 2 * halo
    out_rows = ext_rows - 4
    flops = 2 * epochs * count * epochs * rows * width + 20 * ext_rows * epochs * width
    cost = pl.CostEstimate(
        flops=flops,
        transcendentals=0,
        bytes_accessed=gathered.size * 2 + (out_rows + 2 * halo) * epochs * width * 4,
    )
    return pl.pallas_call(
        _middle_kernel,
        out_shape=jax.ShapeDtypeStruct((out_rows, epochs, width), jnp.float32),
        grid=(rows,),
        in_specs=[
            pl.BlockSpec((count, epochs, epochs), lambda i: (0, 0, 0)),
            pl.BlockSpec((count, None, width, epochs), lambda i: (0, i, 0, 0)),
            pl.BlockSpec((halo, epochs, width), lambda i: (0, 0, 0)),
            pl.BlockSpec((halo, epochs, width), lambda i: (0, 0, 0)),
            pl.BlockSpec((ext_rows - 2, 1, width), lambda i: (0, 0, 0)),
        ],
        out_specs=pl.BlockSpec((out_rows, epochs, width), lambda i: (0, 0, 0)),
        scratch_shapes=[
            pltpu.VMEM((ext_rows, epochs, width), jnp.float32),
            pltpu.VMEM((ext_rows - 2, epochs, width), jnp.float32),
        ],
        compiler_params=pltpu.CompilerParams(
            dimension_semantics=("arbitrary",), vmem_limit_bytes=60 * 1024 * 1024
        ),
        cost_estimate=cost,
    )(lower_e, gathered, top, bottom, gain_rows)


def body(field, factor, kappa):
    epochs, slab, width = field.shape
    count = lax.axis_size("epoch")
    order = epochs * count
    me = lax.axis_index("epoch")
    global_rows = me * epochs + lax.broadcasted_iota(jnp.int32, (epochs, order), 0)
    global_cols = lax.broadcasted_iota(jnp.int32, (epochs, order), 1)
    lower = jnp.where(global_cols <= global_rows, factor, jnp.zeros_like(factor))
    lower = lower.reshape(epochs, count, epochs)
    middle = pinned(jnp.transpose(field[:, EDGE:slab - EDGE], (1, 2, 0)))
    gathered = lax.all_gather(middle, "epoch", axis=0)
    edges = jnp.transpose(
        jnp.concatenate([field[:, :EDGE], field[:, slab - EDGE:]], axis=1), (1, 2, 0)
    )
    slots = [edges]
    for shift in range(1, count):
        pairs = [(e, e + shift) for e in range(count - shift)]
        slots.append(lax.ppermute(edges, "epoch", pairs))
    stacked = jnp.stack(slots, axis=0)
    source = jnp.clip(me - jnp.arange(count), 0, count - 1)
    weights = jnp.take(lower, source, axis=1)
    timed_edges = jnp.einsum("tes,eijs->itj", weights, stacked, preferred_element_type=jnp.float32)
    top, bottom = timed_edges[:EDGE], timed_edges[EDGE:]

    above, below = neighbours(top, bottom, HALO)
    k_above, k_below = neighbours(kappa, kappa, 1)
    gain = jnp.concatenate([k_above, kappa, k_below], axis=0)[:, None, :] + 4.0
    pos = lax.axis_index("row")
    last = lax.axis_size("row") - 1
    out_top = double_stencil(
        jnp.concatenate([above, top], axis=0),
        gain[0:EDGE], gain[1:EDGE - 1], first_outside=pos == 0,
    )
    out_bottom = double_stencil(
        jnp.concatenate([bottom, below], axis=0),
        gain[slab - EDGE + 2:slab + 2], gain[slab - EDGE + 3:slab + 1], last_outside=pos == last,
    )
    out_middle = middle_stencil(
        jnp.transpose(lower, (1, 0, 2)),
        gathered,
        top[EDGE - 2 * HALO:],
        bottom[:2 * HALO],
        gain[EDGE - 2:slab - EDGE + 4],
    )
    product = jnp.concatenate([out_top, out_middle, out_bottom], axis=0)
    return jnp.transpose(product, (1, 0, 2))


def solution(mesh):
    in_specs = (P("epoch", "row", None), P("epoch", None), P("row", None))
    out_specs = P("epoch", "row", None)
    return jax.shard_map(body, mesh=mesh, in_specs=in_specs, out_specs=out_specs, check_vma=False)
```

```python
import jax
import jax.numpy as jnp
from jax import lax
from jax.experimental import pallas as pl
from jax.experimental.pallas import tpu as pltpu
from jax.sharding import PartitionSpec as P

EDGE = 8
HALO = 2


def neighbours(top, bottom, width):
    size = lax.axis_size("row")
    up = [(i, i + 1) for i in range(size - 1)]
    down = [(i + 1, i) for i in range(size - 1)]
    above = lax.ppermute(bottom[bottom.shape[0] - width:], "row", up)
    below = lax.ppermute(top[:width], "row", down)
    return above, below


def side_sum(v):
    padded = jnp.pad(v, [(0, 0)] * (v.ndim - 1) + [(1, 1)])
    return padded[..., :-2] + padded[..., 2:]


def double_stencil(ext, gain_once, gain_out, first_outside=None, last_outside=None):
    once = gain_once * ext[1:-1] - (ext[:-2] + ext[2:] + side_sum(ext[1:-1]))
    if first_outside is not None or last_outside is not None:
        rows = lax.broadcasted_iota(jnp.int32, (once.shape[0], 1, 1), 0)
        outside = jnp.zeros(rows.shape, jnp.bool_)
        if first_outside is not None:
            outside = outside | ((rows == 0) & first_outside)
        if last_outside is not None:
            outside = outside | ((rows == once.shape[0] - 1) & last_outside)
        once = jnp.where(outside, jnp.zeros_like(once), once)
    return gain_out * once[1:-1] - (once[:-2] + once[2:] + side_sum(once[1:-1]))


def _pin_kernel(x_ref, o_ref):
    o_ref[...] = x_ref[...]


def pinned(x):
    return pl.pallas_call(_pin_kernel, out_shape=jax.ShapeDtypeStruct(x.shape, x.dtype))(x)


def _dot_kernel(lower_ref, g_ref, out_ref):
    acc = jnp.zeros(out_ref.shape, jnp.float32)
    for e in range(lower_ref.shape[0]):
        acc = acc + lax.dot_general(
            lower_ref[e], g_ref[e], (((1,), (1,)), ((), ())), preferred_element_type=jnp.float32
        )
    out_ref[...] = acc


def middle_dot(lower_e, gathered):
    count, epochs, _ = lower_e.shape
    _, rows, width, _ = gathered.shape
    cost = pl.CostEstimate(
        flops=2 * epochs * count * epochs * rows * width,
        transcendentals=0,
        bytes_accessed=gathered.size * 2 + rows * epochs * width * 4,
    )
    return pl.pallas_call(
        _dot_kernel,
        out_shape=jax.ShapeDtypeStruct((rows, epochs, width), jnp.float32),
        grid=(rows,),
        in_specs=[
            pl.BlockSpec((count, epochs, epochs), lambda i: (0, 0, 0)),
            pl.BlockSpec((count, None, width, epochs), lambda i: (0, i, 0, 0)),
        ],
        out_specs=pl.BlockSpec((None, epochs, width), lambda i: (i, 0, 0)),
        cost_estimate=cost,
    )(lower_e, gathered)


def body(field, factor, kappa):
    epochs, slab, width = field.shape
    count = lax.axis_size("epoch")
    order = epochs * count
    me = lax.axis_index("epoch")
    global_rows = me * epochs + lax.broadcasted_iota(jnp.int32, (epochs, order), 0)
    global_cols = lax.broadcasted_iota(jnp.int32, (epochs, order), 1)
    lower = jnp.where(global_cols <= global_rows, factor, jnp.zeros_like(factor))
    lower = lower.reshape(epochs, count, epochs)
    middle = pinned(jnp.transpose(field[:, EDGE:slab - EDGE], (1, 2, 0)))
    gathered = lax.all_gather(middle, "epoch", axis=0)
    edges = jnp.transpose(
        jnp.concatenate([field[:, :EDGE], field[:, slab - EDGE:]], axis=1), (1, 2, 0)
    )
    slots = [edges]
    for shift in range(1, count):
        pairs = [(e, e + shift) for e in range(count - shift)]
        slots.append(lax.ppermute(edges, "epoch", pairs))
    stacked = jnp.stack(slots, axis=0)
    source = jnp.clip(me - jnp.arange(count), 0, count - 1)
    weights = jnp.take(lower, source, axis=1)
    timed_edges = jnp.einsum("tes,eijs->itj", weights, stacked, preferred_element_type=jnp.float32)
    top, bottom = timed_edges[:EDGE], timed_edges[EDGE:]

    above, below = neighbours(top, bottom, HALO)
    k_above, k_below = neighbours(kappa, kappa, 1)
    gain = jnp.concatenate([k_above, kappa, k_below], axis=0)[:, None, :] + 4.0
    pos = lax.axis_index("row")
    last = lax.axis_size("row") - 1
    out_top = double_stencil(
        jnp.concatenate([above, top], axis=0),
        gain[0:EDGE], gain[1:EDGE - 1], first_outside=pos == 0,
    )
    out_bottom = double_stencil(
        jnp.concatenate([bottom, below], axis=0),
        gain[slab - EDGE + 2:slab + 2], gain[slab - EDGE + 3:slab + 1], last_outside=pos == last,
    )
    timed_middle = middle_dot(jnp.transpose(lower, (1, 0, 2)), gathered)
    ext = jnp.concatenate([top[EDGE - 2 * HALO:], timed_middle, bottom[:2 * HALO]], axis=0)
    out_middle = double_stencil(ext, gain[EDGE - 2:slab - EDGE + 4], gain[EDGE - 1:slab - EDGE + 3])
    product = jnp.concatenate([out_top, out_middle, out_bottom], axis=0)
    return jnp.transpose(product, (1, 0, 2))


def solution(mesh):
    in_specs = (P("epoch", "row", None), P("epoch", None), P("row", None))
    out_specs = P("epoch", "row", None)
    return jax.shard_map(body, mesh=mesh, in_specs=in_specs, out_specs=out_specs, check_vma=False)
```

```python
import jax
import jax.numpy as jnp
from jax import lax
from jax.experimental import pallas as pl
from jax.experimental.pallas import tpu as pltpu
from jax.sharding import PartitionSpec as P

EDGE = 8
HALO = 2


def neighbours(top, bottom, width):
    size = lax.axis_size("row")
    up = [(i, i + 1) for i in range(size - 1)]
    down = [(i + 1, i) for i in range(size - 1)]
    above = lax.ppermute(bottom[bottom.shape[0] - width:], "row", up)
    below = lax.ppermute(top[:width], "row", down)
    return above, below


def side_sum(v):
    padded = jnp.pad(v, [(0, 0)] * (v.ndim - 1) + [(1, 1)])
    return padded[..., :-2] + padded[..., 2:]


def double_stencil(ext, gain_once, gain_out, first_outside=None, last_outside=None):
    once = gain_once * ext[1:-1] - (ext[:-2] + ext[2:] + side_sum(ext[1:-1]))
    if first_outside is not None or last_outside is not None:
        rows = lax.broadcasted_iota(jnp.int32, (once.shape[0], 1, 1), 0)
        outside = jnp.zeros(rows.shape, jnp.bool_)
        if first_outside is not None:
            outside = outside | ((rows == 0) & first_outside)
        if last_outside is not None:
            outside = outside | ((rows == once.shape[0] - 1) & last_outside)
        once = jnp.where(outside, jnp.zeros_like(once), once)
    return gain_out * once[1:-1] - (once[:-2] + once[2:] + side_sum(once[1:-1]))


def _pin_kernel(x_ref, o_ref):
    o_ref[...] = x_ref[...]


def pinned(x):
    return pl.pallas_call(_pin_kernel, out_shape=jax.ShapeDtypeStruct(x.shape, x.dtype))(x)


def _dot_kernel(lower_ref, g_ref, out_ref):
    for r in range(out_ref.shape[0]):
        acc = jnp.zeros(out_ref.shape[1:], jnp.float32)
        for e in range(lower_ref.shape[0]):
            acc = acc + jnp.dot(g_ref[e, r], lower_ref[e], preferred_element_type=jnp.float32)
        out_ref[r] = acc


def middle_dot(lower_t, gathered, step=2):
    count, _, epochs = lower_t.shape
    _, rows, width, _ = gathered.shape
    cost = pl.CostEstimate(
        flops=2 * epochs * count * epochs * rows * width,
        transcendentals=0,
        bytes_accessed=gathered.size * 2 + rows * epochs * width * 4,
    )
    return pl.pallas_call(
        _dot_kernel,
        out_shape=jax.ShapeDtypeStruct((rows, width, epochs), jnp.float32),
        grid=(rows // step,),
        in_specs=[
            pl.BlockSpec((count, epochs, epochs), lambda i: (0, 0, 0)),
            pl.BlockSpec((count, step, width, epochs), lambda i: (0, i, 0, 0)),
        ],
        out_specs=pl.BlockSpec((step, width, epochs), lambda i: (i, 0, 0)),
        cost_estimate=cost,
    )(lower_t, gathered)


def body(field, factor, kappa):
    epochs, slab, width = field.shape
    count = lax.axis_size("epoch")
    order = epochs * count
    me = lax.axis_index("epoch")
    global_rows = me * epochs + lax.broadcasted_iota(jnp.int32, (epochs, order), 0)
    global_cols = lax.broadcasted_iota(jnp.int32, (epochs, order), 1)
    lower = jnp.where(global_cols <= global_rows, factor, jnp.zeros_like(factor))
    lower = lower.reshape(epochs, count, epochs)
    middle = pinned(jnp.transpose(field[:, EDGE:slab - EDGE], (1, 2, 0)))
    gathered = lax.all_gather(middle, "epoch", axis=0)
    edges = jnp.transpose(
        jnp.concatenate([field[:, :EDGE], field[:, slab - EDGE:]], axis=1), (1, 2, 0)
    )
    slots = [edges]
    for shift in range(1, count):
        pairs = [(e, e + shift) for e in range(count - shift)]
        slots.append(lax.ppermute(edges, "epoch", pairs))
    stacked = jnp.stack(slots, axis=0)
    source = jnp.clip(me - jnp.arange(count), 0, count - 1)
    weights = jnp.take(lower, source, axis=1)
    timed_edges = jnp.einsum("tes,eijs->itj", weights, stacked, preferred_element_type=jnp.float32)
    top, bottom = timed_edges[:EDGE], timed_edges[EDGE:]

    above, below = neighbours(top, bottom, HALO)
    k_above, k_below = neighbours(kappa, kappa, 1)
    gain = jnp.concatenate([k_above, kappa, k_below], axis=0)[:, None, :] + 4.0
    pos = lax.axis_index("row")
    last = lax.axis_size("row") - 1
    out_top = double_stencil(
        jnp.concatenate([above, top], axis=0),
        gain[0:EDGE], gain[1:EDGE - 1], first_outside=pos == 0,
    )
    out_bottom = double_stencil(
        jnp.concatenate([bottom, below], axis=0),
        gain[slab - EDGE + 2:slab + 2], gain[slab - EDGE + 3:slab + 1], last_outside=pos == last,
    )
    timed_middle = jnp.transpose(middle_dot(jnp.transpose(lower, (1, 2, 0)), gathered), (0, 2, 1))
    ext = jnp.concatenate([top[EDGE - 2 * HALO:], timed_middle, bottom[:2 * HALO]], axis=0)
    out_middle = double_stencil(ext, gain[EDGE - 2:slab - EDGE + 4], gain[EDGE - 1:slab - EDGE + 3])
    product = jnp.concatenate([out_top, out_middle, out_bottom], axis=0)
    return jnp.transpose(product, (1, 0, 2))


def solution(mesh):
    in_specs = (P("epoch", "row", None), P("epoch", None), P("row", None))
    out_specs = P("epoch", "row", None)
    return jax.shard_map(body, mesh=mesh, in_specs=in_specs, out_specs=out_specs, check_vma=False)
```

```python
import jax
import jax.numpy as jnp
from jax import lax
from jax.sharding import PartitionSpec as P

EDGE = 8
HALO = 2


def neighbours(top, bottom, width):
    size = lax.axis_size("row")
    up = [(i, i + 1) for i in range(size - 1)]
    down = [(i + 1, i) for i in range(size - 1)]
    above = lax.ppermute(bottom[bottom.shape[0] - width:], "row", up)
    below = lax.ppermute(top[:width], "row", down)
    return above, below


def side_sum(v):
    padded = jnp.pad(v, [(0, 0)] * (v.ndim - 1) + [(1, 1)])
    return padded[..., :-2] + padded[..., 2:]


def double_stencil(ext, gain_once, gain_out, first_outside=None, last_outside=None):
    once = gain_once * ext[1:-1] - (ext[:-2] + ext[2:] + side_sum(ext[1:-1]))
    if first_outside is not None or last_outside is not None:
        rows = lax.broadcasted_iota(jnp.int32, (once.shape[0], 1, 1), 0)
        outside = jnp.zeros(rows.shape, jnp.bool_)
        if first_outside is not None:
            outside = outside | ((rows == 0) & first_outside)
        if last_outside is not None:
            outside = outside | ((rows == once.shape[0] - 1) & last_outside)
        once = jnp.where(outside, jnp.zeros_like(once), once)
    return gain_out * once[1:-1] - (once[:-2] + once[2:] + side_sum(once[1:-1]))


def body(field, factor, kappa):
    epochs, slab, width = field.shape
    count = lax.axis_size("epoch")
    order = epochs * count
    me = lax.axis_index("epoch")
    global_rows = me * epochs + lax.broadcasted_iota(jnp.int32, (epochs, order), 0)
    global_cols = lax.broadcasted_iota(jnp.int32, (epochs, order), 1)
    lower = jnp.where(global_cols <= global_rows, factor, jnp.zeros_like(factor))
    lower = lower.reshape(epochs, count, epochs)
    middle = jnp.transpose(field[:, EDGE:slab - EDGE], (1, 2, 0))
    gathered = lax.all_gather(middle, "epoch", axis=0)
    edges = jnp.transpose(
        jnp.concatenate([field[:, :EDGE], field[:, slab - EDGE:]], axis=1), (1, 2, 0)
    )
    slots = [edges]
    for shift in range(1, count):
        pairs = [(e, e + shift) for e in range(count - shift)]
        halves = [lax.ppermute(edges[h * EDGE:(h + 1) * EDGE], "epoch", pairs) for h in range(2)]
        slots.append(jnp.concatenate(halves, axis=0))
    stacked = jnp.stack(slots, axis=0)
    source = jnp.clip(me - jnp.arange(count), 0, count - 1)
    weights = jnp.take(lower, source, axis=1)
    timed_edges = jnp.einsum("tes,eijs->itj", weights, stacked, preferred_element_type=jnp.float32)
    top, bottom = timed_edges[:EDGE], timed_edges[EDGE:]

    above, below = neighbours(top, bottom, HALO)
    k_above, k_below = neighbours(kappa, kappa, 1)
    gain = jnp.concatenate([k_above, kappa, k_below], axis=0)[:, None, :] + 4.0
    pos = lax.axis_index("row")
    last = lax.axis_size("row") - 1
    out_top = double_stencil(
        jnp.concatenate([above, top], axis=0),
        gain[0:EDGE], gain[1:EDGE - 1], first_outside=pos == 0,
    )
    out_bottom = double_stencil(
        jnp.concatenate([bottom, below], axis=0),
        gain[slab - EDGE + 2:slab + 2], gain[slab - EDGE + 3:slab + 1], last_outside=pos == last,
    )
    timed_middle = jnp.einsum("tes,eijs->itj", lower, gathered, preferred_element_type=jnp.float32)
    ext = jnp.concatenate([top[EDGE - 2 * HALO:], timed_middle, bottom[:2 * HALO]], axis=0)
    out_middle = double_stencil(ext, gain[EDGE - 2:slab - EDGE + 4], gain[EDGE - 1:slab - EDGE + 3])
    product = jnp.concatenate([out_top, out_middle, out_bottom], axis=0)
    return jnp.transpose(product, (1, 0, 2))


def solution(mesh):
    in_specs = (P("epoch", "row", None), P("epoch", None), P("row", None))
    out_specs = P("epoch", "row", None)
    return jax.shard_map(body, mesh=mesh, in_specs=in_specs, out_specs=out_specs, check_vma=False)
```

```python
import jax
import jax.numpy as jnp
from jax import lax
from jax.sharding import Mesh, PartitionSpec as P

EDGE = 8
HALO = 2


def neighbours(top, bottom, width):
    size = lax.axis_size("row")
    up = [(i, i + 1) for i in range(size - 1)]
    down = [(i + 1, i) for i in range(size - 1)]
    above = lax.ppermute(bottom[bottom.shape[0] - width:], "row", up)
    below = lax.ppermute(top[:width], "row", down)
    return above, below


def side_sum(v):
    padded = jnp.pad(v, [(0, 0)] * (v.ndim - 1) + [(1, 1)])
    return padded[..., :-2] + padded[..., 2:]


def double_stencil(ext, gain_once, gain_out, first_outside=None, last_outside=None):
    once = gain_once * ext[1:-1] - (ext[:-2] + ext[2:] + side_sum(ext[1:-1]))
    if first_outside is not None or last_outside is not None:
        rows = lax.broadcasted_iota(jnp.int32, (once.shape[0], 1, 1), 0)
        outside = jnp.zeros(rows.shape, jnp.bool_)
        if first_outside is not None:
            outside = outside | ((rows == 0) & first_outside)
        if last_outside is not None:
            outside = outside | ((rows == once.shape[0] - 1) & last_outside)
        once = jnp.where(outside, jnp.zeros_like(once), once)
    return gain_out * once[1:-1] - (once[:-2] + once[2:] + side_sum(once[1:-1]))


def body(field, factor, kappa):
    epochs, slab, width = field.shape
    planes, sides = lax.axis_size("z"), lax.axis_size("yh")
    count = planes * sides
    order = epochs * count
    me = lax.axis_index("z") * sides + lax.axis_index("yh")
    global_rows = me * epochs + lax.broadcasted_iota(jnp.int32, (epochs, order), 0)
    global_cols = lax.broadcasted_iota(jnp.int32, (epochs, order), 1)
    lower = jnp.where(global_cols <= global_rows, factor, jnp.zeros_like(factor))
    lower = lower.reshape(epochs, count, epochs)
    middle = jnp.transpose(field[:, EDGE:slab - EDGE], (1, 2, 0))
    pair = lax.all_gather(middle, "yh", axis=0)
    gathered = lax.all_gather(pair, "z", axis=0).reshape((count,) + middle.shape)
    edges = jnp.transpose(
        jnp.concatenate([field[:, :EDGE], field[:, slab - EDGE:]], axis=1), (1, 2, 0)
    )
    slots = [edges]
    for shift in range(1, count):
        pairs = [(e, e + shift) for e in range(count - shift)]
        slots.append(lax.ppermute(edges, ("z", "yh"), pairs))
    stacked = jnp.stack(slots, axis=0)
    source = jnp.clip(me - jnp.arange(count), 0, count - 1)
    weights = jnp.take(lower, source, axis=1)
    timed_edges = jnp.einsum("tes,eijs->itj", weights, stacked, preferred_element_type=jnp.float32)
    top, bottom = timed_edges[:EDGE], timed_edges[EDGE:]

    above, below = neighbours(top, bottom, HALO)
    k_above, k_below = neighbours(kappa, kappa, 1)
    gain = jnp.concatenate([k_above, kappa, k_below], axis=0)[:, None, :] + 4.0
    pos = lax.axis_index("row")
    last = lax.axis_size("row") - 1
    out_top = double_stencil(
        jnp.concatenate([above, top], axis=0),
        gain[0:EDGE], gain[1:EDGE - 1], first_outside=pos == 0,
    )
    out_bottom = double_stencil(
        jnp.concatenate([bottom, below], axis=0),
        gain[slab - EDGE + 2:slab + 2], gain[slab - EDGE + 3:slab + 1], last_outside=pos == last,
    )
    timed_middle = jnp.einsum("tes,eijs->itj", lower, gathered, preferred_element_type=jnp.float32)
    ext = jnp.concatenate([top[EDGE - 2 * HALO:], timed_middle, bottom[:2 * HALO]], axis=0)
    out_middle = double_stencil(ext, gain[EDGE - 2:slab - EDGE + 4], gain[EDGE - 1:slab - EDGE + 3])
    product = jnp.concatenate([out_top, out_middle, out_bottom], axis=0)
    return jnp.transpose(product, (1, 0, 2))


def solution(mesh):
    devices = mesh.devices
    planes = 4 if devices.shape[0] % 4 == 0 else 1
    view = Mesh(
        devices.reshape(planes, devices.shape[0] // planes, devices.shape[1]), ("z", "yh", "row")
    )
    epoch = ("z", "yh")
    in_specs = (P(epoch, "row", None), P(epoch, None), P("row", None))
    out_specs = P(epoch, "row", None)
    return jax.shard_map(body, mesh=view, in_specs=in_specs, out_specs=out_specs, check_vma=False)
```

```python
import jax
import jax.numpy as jnp
from jax import lax
from jax.sharding import PartitionSpec as P

EDGE = 6
HALO = 2


def neighbours(top, bottom, width):
    size = lax.axis_size("row")
    up = [(i, i + 1) for i in range(size - 1)]
    down = [(i + 1, i) for i in range(size - 1)]
    above = lax.ppermute(bottom[bottom.shape[0] - width:], "row", up)
    below = lax.ppermute(top[:width], "row", down)
    return above, below


def side_sum(v):
    padded = jnp.pad(v, [(0, 0)] * (v.ndim - 1) + [(1, 1)])
    return padded[..., :-2] + padded[..., 2:]


def double_stencil(ext, gain_once, gain_out, first_outside=None, last_outside=None):
    once = gain_once * ext[1:-1] - (ext[:-2] + ext[2:] + side_sum(ext[1:-1]))
    if first_outside is not None or last_outside is not None:
        rows = lax.broadcasted_iota(jnp.int32, (once.shape[0], 1, 1), 0)
        outside = jnp.zeros(rows.shape, jnp.bool_)
        if first_outside is not None:
            outside = outside | ((rows == 0) & first_outside)
        if last_outside is not None:
            outside = outside | ((rows == once.shape[0] - 1) & last_outside)
        once = jnp.where(outside, jnp.zeros_like(once), once)
    return gain_out * once[1:-1] - (once[:-2] + once[2:] + side_sum(once[1:-1]))


def body(field, factor, kappa):
    epochs, slab, width = field.shape
    count = lax.axis_size("epoch")
    order = epochs * count
    me = lax.axis_index("epoch")
    global_rows = me * epochs + lax.broadcasted_iota(jnp.int32, (epochs, order), 0)
    global_cols = lax.broadcasted_iota(jnp.int32, (epochs, order), 1)
    lower = jnp.where(global_cols <= global_rows, factor, jnp.zeros_like(factor))
    lower = lower.reshape(epochs, count, epochs)
    middle = jnp.transpose(field[:, EDGE:slab - EDGE], (1, 2, 0))
    gathered = lax.all_gather(middle, "epoch", axis=0)
    edges = jnp.transpose(
        jnp.concatenate([field[:, :EDGE], field[:, slab - EDGE:]], axis=1), (1, 2, 0)
    )
    slots = [edges]
    for shift in range(1, count):
        pairs = [(e, e + shift) for e in range(count - shift)]
        slots.append(lax.ppermute(edges, "epoch", pairs))
    stacked = jnp.stack(slots, axis=0)
    source = jnp.clip(me - jnp.arange(count), 0, count - 1)
    weights = jnp.take(lower, source, axis=1)
    timed_edges = jnp.einsum("tes,eijs->itj", weights, stacked, preferred_element_type=jnp.float32)
    top, bottom = timed_edges[:EDGE], timed_edges[EDGE:]

    above, below = neighbours(top, bottom, HALO)
    k_above, k_below = neighbours(kappa, kappa, 1)
    gain = jnp.concatenate([k_above, kappa, k_below], axis=0)[:, None, :] + 4.0
    pos = lax.axis_index("row")
    last = lax.axis_size("row") - 1
    out_top = double_stencil(
        jnp.concatenate([above, top], axis=0),
        gain[0:EDGE], gain[1:EDGE - 1], first_outside=pos == 0,
    )
    out_bottom = double_stencil(
        jnp.concatenate([bottom, below], axis=0),
        gain[slab - EDGE + 2:slab + 2], gain[slab - EDGE + 3:slab + 1], last_outside=pos == last,
    )
    timed_middle = jnp.einsum("tes,eijs->itj", lower, gathered, preferred_element_type=jnp.float32)
    ext = jnp.concatenate([top[EDGE - 2 * HALO:], timed_middle, bottom[:2 * HALO]], axis=0)
    out_middle = double_stencil(ext, gain[EDGE - 2:slab - EDGE + 4], gain[EDGE - 1:slab - EDGE + 3])
    product = jnp.concatenate([out_top, out_middle, out_bottom], axis=0)
    return jnp.transpose(product, (1, 0, 2))


def solution(mesh):
    in_specs = (P("epoch", "row", None), P("epoch", None), P("row", None))
    out_specs = P("epoch", "row", None)
    return jax.shard_map(body, mesh=mesh, in_specs=in_specs, out_specs=out_specs, check_vma=False)
```

```python
import jax
import jax.numpy as jnp
from jax import lax
from jax.sharding import PartitionSpec as P

EDGE = 8
HALO = 2


def neighbours(top, bottom, width):
    size = lax.axis_size("row")
    up = [(i, i + 1) for i in range(size - 1)]
    down = [(i + 1, i) for i in range(size - 1)]
    above = lax.ppermute(bottom[bottom.shape[0] - width:], "row", up)
    below = lax.ppermute(top[:width], "row", down)
    return above, below


def side_sum(v):
    padded = jnp.pad(v, [(0, 0)] * (v.ndim - 1) + [(1, 1)])
    return padded[..., :-2] + padded[..., 2:]


def double_stencil(ext, gain_once, gain_out, first_outside=None, last_outside=None):
    once = gain_once * ext[1:-1] - (ext[:-2] + ext[2:] + side_sum(ext[1:-1]))
    if first_outside is not None or last_outside is not None:
        rows = lax.broadcasted_iota(jnp.int32, (once.shape[0], 1, 1), 0)
        outside = jnp.zeros(rows.shape, jnp.bool_)
        if first_outside is not None:
            outside = outside | ((rows == 0) & first_outside)
        if last_outside is not None:
            outside = outside | ((rows == once.shape[0] - 1) & last_outside)
        once = jnp.where(outside, jnp.zeros_like(once), once)
    return gain_out * once[1:-1] - (once[:-2] + once[2:] + side_sum(once[1:-1]))


def body(field, factor, kappa):
    epochs, slab, width = field.shape
    count = lax.axis_size("epoch")
    order = epochs * count
    me = lax.axis_index("epoch")
    global_rows = me * epochs + lax.broadcasted_iota(jnp.int32, (epochs, order), 0)
    global_cols = lax.broadcasted_iota(jnp.int32, (epochs, order), 1)
    lower = jnp.where(global_cols <= global_rows, factor, jnp.zeros_like(factor))
    lower = lower.reshape(epochs, count, epochs)
    middle = jnp.transpose(field[:, EDGE:slab - EDGE], (1, 2, 0))
    gathered = lax.all_gather(middle, "epoch", axis=2, tiled=True)
    edges = jnp.transpose(
        jnp.concatenate([field[:, :EDGE], field[:, slab - EDGE:]], axis=1), (1, 2, 0)
    )
    slots = [edges]
    for shift in range(1, count):
        pairs = [(e, e + shift) for e in range(count - shift)]
        slots.append(lax.ppermute(edges, "epoch", pairs))
    stacked = jnp.stack(slots, axis=0)
    source = jnp.clip(me - jnp.arange(count), 0, count - 1)
    weights = jnp.take(lower, source, axis=1)
    timed_edges = jnp.einsum("tes,eijs->itj", weights, stacked, preferred_element_type=jnp.float32)
    top, bottom = timed_edges[:EDGE], timed_edges[EDGE:]

    above, below = neighbours(top, bottom, HALO)
    k_above, k_below = neighbours(kappa, kappa, 1)
    gain = jnp.concatenate([k_above, kappa, k_below], axis=0)[:, None, :] + 4.0
    pos = lax.axis_index("row")
    last = lax.axis_size("row") - 1
    out_top = double_stencil(
        jnp.concatenate([above, top], axis=0),
        gain[0:EDGE], gain[1:EDGE - 1], first_outside=pos == 0,
    )
    out_bottom = double_stencil(
        jnp.concatenate([bottom, below], axis=0),
        gain[slab - EDGE + 2:slab + 2], gain[slab - EDGE + 3:slab + 1], last_outside=pos == last,
    )
    timed_middle = jnp.einsum(
        "tk,ijk->itj", lower.reshape(epochs, order), gathered, preferred_element_type=jnp.float32
    )
    ext = jnp.concatenate([top[EDGE - 2 * HALO:], timed_middle, bottom[:2 * HALO]], axis=0)
    out_middle = double_stencil(ext, gain[EDGE - 2:slab - EDGE + 4], gain[EDGE - 1:slab - EDGE + 3])
    product = jnp.concatenate([out_top, out_middle, out_bottom], axis=0)
    return jnp.transpose(product, (1, 0, 2))


def solution(mesh):
    in_specs = (P("epoch", "row", None), P("epoch", None), P("row", None))
    out_specs = P("epoch", "row", None)
    return jax.shard_map(body, mesh=mesh, in_specs=in_specs, out_specs=out_specs, check_vma=False)
```

```python
import jax
import jax.numpy as jnp
from jax import lax
from jax.sharding import PartitionSpec as P

EDGE = 9
HALO = 2


def neighbours(top, bottom, width):
    size = lax.axis_size("row")
    up = [(i, i + 1) for i in range(size - 1)]
    down = [(i + 1, i) for i in range(size - 1)]
    above = lax.ppermute(bottom[bottom.shape[0] - width:], "row", up)
    below = lax.ppermute(top[:width], "row", down)
    return above, below


def side_sum(v):
    padded = jnp.pad(v, [(0, 0)] * (v.ndim - 1) + [(1, 1)])
    return padded[..., :-2] + padded[..., 2:]


def double_stencil(ext, gain_once, gain_out, first_outside=None, last_outside=None):
    once = gain_once * ext[1:-1] - (ext[:-2] + ext[2:] + side_sum(ext[1:-1]))
    if first_outside is not None or last_outside is not None:
        rows = lax.broadcasted_iota(jnp.int32, (once.shape[0], 1, 1), 0)
        outside = jnp.zeros(rows.shape, jnp.bool_)
        if first_outside is not None:
            outside = outside | ((rows == 0) & first_outside)
        if last_outside is not None:
            outside = outside | ((rows == once.shape[0] - 1) & last_outside)
        once = jnp.where(outside, jnp.zeros_like(once), once)
    return gain_out * once[1:-1] - (once[:-2] + once[2:] + side_sum(once[1:-1]))


def body(field, factor, kappa):
    epochs, slab, width = field.shape
    count = lax.axis_size("epoch")
    order = epochs * count
    me = lax.axis_index("epoch")
    global_rows = me * epochs + lax.broadcasted_iota(jnp.int32, (epochs, order), 0)
    global_cols = lax.broadcasted_iota(jnp.int32, (epochs, order), 1)
    lower = jnp.where(global_cols <= global_rows, factor, jnp.zeros_like(factor))
    lower = lower.reshape(epochs, count, epochs)
    middle = jnp.transpose(field[:, EDGE:slab - EDGE], (1, 2, 0))
    gathered = lax.all_gather(middle, "epoch", axis=0)
    edges = jnp.transpose(
        jnp.concatenate([field[:, :EDGE], field[:, slab - EDGE:]], axis=1), (1, 2, 0)
    )
    slots = [edges]
    for shift in range(1, count):
        pairs = [(e, e + shift) for e in range(count - shift)]
        slots.append(lax.ppermute(edges, "epoch", pairs))
    stacked = jnp.stack(slots, axis=0)
    source = jnp.clip(me - jnp.arange(count), 0, count - 1)
    weights = jnp.take(lower, source, axis=1)
    timed_edges = jnp.einsum("tes,eijs->itj", weights, stacked, preferred_element_type=jnp.float32)
    top, bottom = timed_edges[:EDGE], timed_edges[EDGE:]

    above, below = neighbours(top, bottom, HALO)
    k_above, k_below = neighbours(kappa, kappa, 1)
    gain = jnp.concatenate([k_above, kappa, k_below], axis=0)[:, None, :] + 4.0
    pos = lax.axis_index("row")
    last = lax.axis_size("row") - 1
    out_top = double_stencil(
        jnp.concatenate([above, top], axis=0),
        gain[0:EDGE], gain[1:EDGE - 1], first_outside=pos == 0,
    )
    out_bottom = double_stencil(
        jnp.concatenate([bottom, below], axis=0),
        gain[slab - EDGE + 2:slab + 2], gain[slab - EDGE + 3:slab + 1], last_outside=pos == last,
    )
    timed_middle = jnp.einsum("tes,eijs->itj", lower, gathered, preferred_element_type=jnp.float32)
    ext = jnp.concatenate([top[EDGE - 2 * HALO:], timed_middle, bottom[:2 * HALO]], axis=0)
    out_middle = double_stencil(ext, gain[EDGE - 2:slab - EDGE + 4], gain[EDGE - 1:slab - EDGE + 3])
    product = jnp.concatenate([out_top, out_middle, out_bottom], axis=0)
    return jnp.transpose(product, (1, 0, 2))


def solution(mesh):
    in_specs = (P("epoch", "row", None), P("epoch", None), P("row", None))
    out_specs = P("epoch", "row", None)
    return jax.shard_map(body, mesh=mesh, in_specs=in_specs, out_specs=out_specs, check_vma=False)
```

```python
import jax
import jax.numpy as jnp
from jax import lax
from jax.sharding import PartitionSpec as P

EDGE = 8
HALO = 2


def neighbours(top, bottom, width):
    size = lax.axis_size("row")
    up = [(i, i + 1) for i in range(size - 1)]
    down = [(i + 1, i) for i in range(size - 1)]
    above = lax.ppermute(bottom[bottom.shape[0] - width:], "row", up)
    below = lax.ppermute(top[:width], "row", down)
    return above, below


def side_sum(v):
    padded = jnp.pad(v, [(0, 0)] * (v.ndim - 1) + [(1, 1)])
    return padded[..., :-2] + padded[..., 2:]


def double_stencil(ext, gain_once, gain_out, first_outside=None, last_outside=None):
    once = gain_once * ext[1:-1] - (ext[:-2] + ext[2:] + side_sum(ext[1:-1]))
    if first_outside is not None or last_outside is not None:
        rows = lax.broadcasted_iota(jnp.int32, (once.shape[0], 1, 1), 0)
        outside = jnp.zeros(rows.shape, jnp.bool_)
        if first_outside is not None:
            outside = outside | ((rows == 0) & first_outside)
        if last_outside is not None:
            outside = outside | ((rows == once.shape[0] - 1) & last_outside)
        once = jnp.where(outside, jnp.zeros_like(once), once)
    return gain_out * once[1:-1] - (once[:-2] + once[2:] + side_sum(once[1:-1]))


def body(field, factor, kappa):
    epochs, slab, width = field.shape
    count = lax.axis_size("epoch")
    order = epochs * count
    me = lax.axis_index("epoch")
    global_rows = me * epochs + lax.broadcasted_iota(jnp.int32, (epochs, order), 0)
    global_cols = lax.broadcasted_iota(jnp.int32, (epochs, order), 1)
    lower = jnp.where(global_cols <= global_rows, factor, jnp.zeros_like(factor))
    lower = lower.reshape(epochs, count, epochs)
    middle = jnp.transpose(field[:, EDGE:slab - EDGE], (1, 2, 0))
    gathered = lax.all_gather(middle, "epoch", axis=0)
    edges = jnp.transpose(
        jnp.concatenate([field[:, :EDGE], field[:, slab - EDGE:]], axis=1), (1, 2, 0)
    )
    slots = [edges]
    for shift in range(1, count):
        pairs = [(e, e + shift) for e in range(count - shift)]
        slots.append(lax.ppermute(edges, "epoch", pairs))
    stacked = jnp.stack(slots, axis=0)
    source = jnp.clip(me - jnp.arange(count), 0, count - 1)
    weights = jnp.take(lower, source, axis=1)
    timed_edges = jnp.einsum("tes,eijs->itj", weights, stacked, preferred_element_type=jnp.float32)
    top, bottom = timed_edges[:EDGE], timed_edges[EDGE:]

    above, below = neighbours(top, bottom, HALO)
    k_above, k_below = neighbours(kappa, kappa, 1)
    gain = jnp.concatenate([k_above, kappa, k_below], axis=0)[:, None, :] + 4.0
    pos = lax.axis_index("row")
    last = lax.axis_size("row") - 1
    out_top = double_stencil(
        jnp.concatenate([above, top], axis=0),
        gain[0:EDGE], gain[1:EDGE - 1], first_outside=pos == 0,
    )
    out_bottom = double_stencil(
        jnp.concatenate([bottom, below], axis=0),
        gain[slab - EDGE + 2:slab + 2], gain[slab - EDGE + 3:slab + 1], last_outside=pos == last,
    )
    timed_middle = jnp.einsum("tes,eijs->itj", lower, gathered, preferred_element_type=jnp.float32)
    frame = jnp.concatenate(
        [top[EDGE - 2 * HALO:], jnp.zeros_like(timed_middle), bottom[:2 * HALO]], axis=0
    )
    ext = lax.dynamic_update_slice_in_dim(frame, timed_middle, 2 * HALO, 0)
    out_middle = double_stencil(ext, gain[EDGE - 2:slab - EDGE + 4], gain[EDGE - 1:slab - EDGE + 3])
    product = jnp.concatenate([out_top, out_middle, out_bottom], axis=0)
    return jnp.transpose(product, (1, 0, 2))


def solution(mesh):
    in_specs = (P("epoch", "row", None), P("epoch", None), P("row", None))
    out_specs = P("epoch", "row", None)
    return jax.shard_map(body, mesh=mesh, in_specs=in_specs, out_specs=out_specs, check_vma=False)
```
